256 devices in a mesh: dp: 16 (over y, z_hi, core), tensor: 16 (over z_lo, x).
Axes of the slice: x: 4, y: 4, z: 8 (z_hi: 2, z_lo: 4; z = z_hi * 4 + z_lo), core: 2. Of those that a mesh axis runs over, the one named last changes fastest.
Arguments:
- token_ids: int32 [4096], P('dp'), may hold values from 0 to 128255
- attn_heads: bfloat16 [4096, 8192], P('dp', 'tensor'), may hold values from -6 to 6
- out_proj: bfloat16 [8192, 8192], P('tensor'), may hold values from -0.0625 to 0.0625
- residual: bfloat16 [4096, 8192], P(('dp', 'tensor')), may hold values from -6 to 6
- norm_gain: float32 [8192], replicated, may hold values from 0.5 to 1.5
- twist_in: bfloat16 [8192, 8192], P('dp', 'tensor'), may hold values from -0.0625 to 0.0625
- twist_out: float32 [8192], P('tensor'), may hold values from -0.26516503 to 0.26516503
- token_bias: float32 [128256], replicated, may hold values from -4 to 262
- toxicity: int32 [16], P('dp'), may hold values from 1 to 4
- prompt_len: int32 [16], P('dp'), may hold values from 1 to 128
Outputs:
- twist_vals: float32 [4096], P('dp')
- grad_in: float32 [8192, 8192], P('dp', 'tensor')
- grad_out: float32 [8192], P('tensor')
- grad_bias: float32 [128256], P('dp')
The draws below stay inside these ranges and needn't reach their ends.
All inputs are finite; a program needn't handle non-finite values.
Results may differ from the reference program's by a relative error of at most 0.033.
Values may be sent and summed in bfloat16 or wider, within the bound.
No kernel may reach another device: no remote copies, remote signals or barrier semaphores. Data moves between devices by JAX's collectives and lax.ppermute only.
A program may use at most 128 MiB of HBM per device.

```python
import math
import jax
import jax.numpy as jnp
import numpy as np
from jax import lax

D = 8192
VOCAB = 128256
LEN = 256
ROLLOUTS = 16
TOKENS = 4096
N_DP = 16
N_TENSOR = 16


def draw_token_bias(key, part):
    key_one = jax.random.fold_in(key, 0)
    return jnp.clip(jax.random.normal(key_one, (VOCAB,), jnp.float32), -4.0, 4.0)


def with_ends(result, stream_key, least, high):
    spot = [jax.random.randint(jax.random.fold_in(stream_key, axis), (), 0, length) for axis, length in enumerate(result.shape)]
    longest = result.shape.index(max(result.shape))
    beside = spot[:longest] + [(spot[longest] + 1) % result.shape[longest]] + spot[longest + 1:]
    return result.at[tuple(spot)].set(least).at[tuple(beside)].set(high)


def shard_levels(key, dims, shards, smallest, top_value):
    def one(axis_at, parts):
        heights = jax.random.uniform(jax.random.fold_in(jax.random.fold_in(key, 6), axis_at), (parts,), jnp.float32, smallest / len(shards), top_value / len(shards))
        return jnp.repeat(jnp.exp(heights), dims[axis_at] // parts).reshape((-1,) + (1,) * (len(dims) - axis_at - 1))

    factor_of = one(*shards[0])
    for cut in shards[1:]:
        factor_of = factor_of * one(*cut)
    return factor_of


def wide_ids(rng, shape, number_of, skew):
    loads = [min(1 << octave, number_of + 1 - (1 << octave)) * (1 << 20) // math.isqrt((1 << octave) ** skew) + 1 for octave in range((number_of + 1).bit_length()) if 1 << octave <= number_of]
    scale = 1 + sum(loads) // (1 << 30)
    table = np.cumsum(np.array([max(1, weight // scale) for weight in loads]))
    ticket = jax.random.randint(jax.random.fold_in(rng, 1), shape, 0, int(table[len(loads) - 1]))
    start = jnp.left_shift(1, jnp.searchsorted(jnp.asarray(table, jnp.int32), ticket, side="right").astype(jnp.int32))
    grade = start - 1 + jax.random.randint(jax.random.fold_in(rng, 4), shape, 0, 1 << 30) % jnp.minimum(start, number_of + 1 - start)
    return jax.random.permutation(jax.random.fold_in(rng, 2), number_of)[grade].astype(jnp.int32)


def bell_draw(stream_key, shape, scale, bound, cuts=(), dtype=jnp.bfloat16):
    drawn = scale * jax.random.normal(stream_key, shape, jnp.float32)
    if cuts:
        drawn = drawn * shard_levels(stream_key, shape, cuts, -0.22, 0.18)
    return jnp.clip(drawn, -bound, bound).astype(dtype)


def setup_inputs(seed: int = 0) -> dict:
    splits = jax.random.split(jax.random.key(seed), 11)
    return {
        "token_ids": with_ends(wide_ids(splits[0], (TOKENS,), VOCAB, 2), jax.random.fold_in(splits[0], 3), 0, VOCAB - 1).astype(jnp.int32),
        "attn_heads": bell_draw(splits[1], (TOKENS, D), 1.0, 6.0, ((0, 16), (1, 16))),
        "out_proj": bell_draw(splits[2], (D, D), D ** -0.5, 0.0625, ((0, 16),)),
        "residual": bell_draw(splits[3], (TOKENS, D), 1.0, 6.0, ((0, 256),)),
        "norm_gain": jnp.clip(1.0 + 0.1 * jax.random.normal(splits[4], (D,), jnp.float32), 0.5, 1.5),
        "twist_in": bell_draw(splits[5], (D, D), D ** -0.5, 0.0625, ((0, 16), (1, 16))),
        "twist_out": bell_draw(splits[6], (D,), (4.0 / D ** 0.5), 0.26516503, ((0, 16),), jnp.float32),
        "token_bias": draw_token_bias(jax.random.fold_in(splits[10], 71), 0),
        "toxicity": with_ends(jax.random.randint(splits[8], (ROLLOUTS,), 1, 5), jax.random.fold_in(splits[8], 1), 1, 4).astype(jnp.int32),
        "prompt_len": with_ends(jax.random.randint(splits[9], (ROLLOUTS,), 1, LEN // 2 + 1), jax.random.fold_in(splits[9], 1), 1, (LEN // 2 + 1) - 1).astype(jnp.int32),
    }


def normalize(hidden, norm_gain):
    values = hidden.astype(jnp.float32)
    scaled = lax.rsqrt(lax.optimization_barrier(jnp.mean(values * values, axis=-1, keepdims=True)) + 1e-05)
    return (values * scaled * norm_gain[None, :]).astype(jnp.bfloat16)

def reference(token_ids, attn_heads, out_proj, residual, norm_gain, twist_in, twist_out, token_bias, toxicity, prompt_len):
    block_width = D // N_TENSOR
    tok_count = attn_heads.shape[0]
    head_blocks = attn_heads.reshape(tok_count, N_TENSOR, block_width).transpose(1, 0, 2)
    proj_blocks = out_proj.reshape(N_TENSOR, block_width, D)

    def add_block(accum, pair):
        partial_sum = jnp.dot(pair[0], pair[1], preferred_element_type=jnp.float32).astype(jnp.bfloat16)
        partial_sum = lax.optimization_barrier(partial_sum)
        return (accum + partial_sum.astype(jnp.float32), None)
    summed, unused = lax.scan(add_block, jnp.zeros((tok_count, D), jnp.float32), (head_blocks, proj_blocks))
    hidden = (residual.astype(jnp.float32) + summed).astype(jnp.bfloat16)
    normed = normalize(hidden, norm_gain)
    pre_act = jnp.dot(normed, twist_in, preferred_element_type=jnp.float32)
    active = jax.nn.silu(pre_act)
    twist_vals = jnp.dot(active, twist_out, precision=lax.Precision.HIGHEST) + token_bias[token_ids]
    grid = twist_vals.reshape(N_DP, LEN)
    live = jnp.arange(LEN)[None, :] >= prompt_len[:, None]
    levels = toxicity.astype(jnp.float32)[:, None] * live.astype(jnp.float32)
    highest = lax.optimization_barrier(jnp.max(jnp.where(live, grid, -1e+30), axis=0))
    expo = jnp.where(live, jnp.exp(jnp.where(live, grid - highest[None, :], -80.0)), 0.0)
    totals = lax.optimization_barrier(jnp.sum(expo, axis=0))
    lab_sum = lax.optimization_barrier(jnp.sum(levels, axis=0))
    weights = (expo / jnp.maximum(totals, 1.0)[None, :] - levels / jnp.maximum(lab_sum, 1.0)[None, :]) / LEN
    flat = weights.reshape(-1)
    grad_out = jnp.dot(flat, active, precision=lax.Precision.HIGHEST)
    grad_bias = jax.ops.segment_sum(flat, token_ids, num_segments=VOCAB)
    sigma = jax.nn.sigmoid(pre_act)
    d_pre = (flat[:, None] * twist_out[None, :] * sigma * (1.0 + pre_act * (1.0 - sigma))).astype(jnp.bfloat16)
    grad_in = jnp.dot(normed.T, d_pre, preferred_element_type=jnp.float32)
    return (twist_vals, grad_in, grad_out, grad_bias)
```

```python
import jax
import jax.numpy as jnp
from jax import lax
from jax.sharding import PartitionSpec as P


def normalize(hidden, norm_gain):
    values = hidden.astype(jnp.float32)
    scaled = lax.rsqrt(jnp.mean(values * values, axis=-1, keepdims=True) + 1e-05)
    return (values * scaled * norm_gain[None, :]).astype(jnp.bfloat16)


def local(
    token_ids,
    attn_heads,
    out_proj,
    residual,
    norm_gain,
    twist_in,
    twist_out,
    token_bias,
    toxicity,
    prompt_len,
):
    seq_len = attn_heads.shape[0]
    vocab_size = token_bias.shape[0]
    n_dp = lax.axis_size("dp")
    r = lax.axis_index("dp")

    ints = jnp.concatenate([token_ids, prompt_len, toxicity])
    ints_all = lax.all_gather(ints, "dp", axis=0)
    ids_all = ints_all[:, :seq_len]
    plen_all = ints_all[:, seq_len]
    tox_all = ints_all[:, seq_len + 1]

    twist_full = lax.all_gather(twist_in, "dp", axis=0, tiled=True)

    partial_sum = jnp.dot(attn_heads, out_proj, preferred_element_type=jnp.float32)
    summed = lax.psum_scatter(
        partial_sum.astype(jnp.bfloat16), "tensor", scatter_dimension=0, tiled=True
    ).astype(jnp.float32)
    hidden = (residual.astype(jnp.float32) + summed).astype(jnp.bfloat16)
    normed_rows = normalize(hidden, norm_gain)
    normed = lax.all_gather(normed_rows, "tensor", axis=0, tiled=True)

    pre_act = jnp.dot(normed, twist_full, preferred_element_type=jnp.float32)
    active = jax.nn.silu(pre_act)
    partial_psi = jnp.dot(active, twist_out, precision=lax.Precision.HIGHEST)
    slot = (jnp.arange(n_dp) == r).astype(jnp.float32)
    psi_all = lax.psum(slot[:, None] * partial_psi[None, :], ("dp", "tensor"))
    grid = psi_all + token_bias[ids_all]

    live = jnp.arange(seq_len)[None, :] >= plen_all[:, None]
    levels = tox_all.astype(jnp.float32)[:, None] * live.astype(jnp.float32)
    highest = jnp.max(jnp.where(live, grid, -1e30), axis=0)
    expo = jnp.where(live, jnp.exp(jnp.where(live, grid - highest[None, :], -80.0)), 0.0)
    totals = jnp.sum(expo, axis=0)
    lab_sum = jnp.sum(levels, axis=0)
    weights_all = (
        expo / jnp.maximum(totals, 1.0)[None, :] - levels / jnp.maximum(lab_sum, 1.0)[None, :]
    ) / seq_len

    twist_vals = lax.dynamic_index_in_dim(grid, r, axis=0, keepdims=False)
    weights = lax.dynamic_index_in_dim(weights_all, r, axis=0, keepdims=False)

    grad_out = lax.psum(jnp.dot(weights, active, precision=lax.Precision.HIGHEST), "dp")

    slice_len = vocab_size // n_dp
    idx = ids_all.reshape(-1) - r * slice_len
    idx = jnp.where((idx >= 0) & (idx < slice_len), idx, slice_len)
    grad_bias = jnp.zeros((slice_len,), jnp.float32).at[idx].add(
        weights_all.reshape(-1), mode="drop"
    )

    sigma = jax.nn.sigmoid(pre_act)
    d_pre = (
        weights[:, None] * twist_out[None, :] * sigma * (1.0 + pre_act * (1.0 - sigma))
    ).astype(jnp.bfloat16)
    contract = (((0,), (0,)), ((), ()))
    grad_in = lax.psum_scatter(
        lax.dot_general(normed, d_pre, contract, preferred_element_type=jnp.float32).astype(
            jnp.bfloat16
        ),
        "dp",
        scatter_dimension=0,
        tiled=True,
    ).astype(jnp.float32)
    return (twist_vals, grad_in, grad_out, grad_bias)


def solution(mesh):
    placed = (
        P("dp"),
        P("dp", "tensor"),
        P("tensor", None),
        P(("dp", "tensor"), None),
        P(),
        P("dp", "tensor"),
        P("tensor"),
        P(),
        P("dp"),
        P("dp"),
    )
    return jax.shard_map(
        local,
        mesh=mesh,
        in_specs=placed,
        out_specs=(P("dp"), P("dp", "tensor"), P("tensor"), P("dp")),
        check_vma=False,
    )
```

```python
import jax
import jax.numpy as jnp
from jax import lax
from jax.sharding import PartitionSpec as P

SPLITS = 1


def normalize(hidden, norm_gain):
    values = hidden.astype(jnp.float32)
    scaled = lax.rsqrt(jnp.mean(values * values, axis=-1, keepdims=True) + 1e-05)
    return (values * scaled * norm_gain[None, :]).astype(jnp.bfloat16)


def local(
    token_ids,
    attn_heads,
    out_proj,
    residual,
    norm_gain,
    twist_in,
    twist_out,
    token_bias,
    toxicity,
    prompt_len,
):
    seq_len = attn_heads.shape[0]
    width = out_proj.shape[1]
    vocab_size = token_bias.shape[0]
    n_dp = lax.axis_size("dp")
    r = lax.axis_index("dp")
    j = lax.axis_index("tensor")
    rows = residual.shape[0]

    twist_full = lax.all_gather(twist_in, "dp", axis=0, tiled=True)

    resid_pad = lax.dynamic_update_slice(
        jnp.zeros((seq_len, width), residual.dtype), residual, (j * rows, 0)
    )
    partial_sum = jnp.dot(attn_heads, out_proj, preferred_element_type=jnp.float32)
    partial_sum = (partial_sum + resid_pad.astype(jnp.float32)).astype(jnp.bfloat16)
    cut = width // SPLITS
    hidden = jnp.concatenate(
        [lax.psum(partial_sum[:, s * cut:(s + 1) * cut], "tensor") for s in range(SPLITS)],
        axis=1,
    )
    normed = normalize(hidden, norm_gain)

    pre_act = jnp.dot(normed, twist_full, preferred_element_type=jnp.float32)
    active = jax.nn.silu(pre_act)
    partial_psi = jnp.dot(active, twist_out, precision=lax.Precision.HIGHEST)

    lead = (j == 0).astype(jnp.float32)
    own_bias = token_bias[token_ids]
    row = jnp.concatenate(
        [
            partial_psi + lead * own_bias,
            lead * token_ids.astype(jnp.float32),
            lead * prompt_len.astype(jnp.float32),
            lead * toxicity.astype(jnp.float32),
        ]
    )
    slot = (jnp.arange(n_dp) == r).astype(jnp.float32)
    slab = lax.psum(slot[:, None] * row[None, :], ("dp", "tensor"))
    grid = slab[:, :seq_len]
    ids_all = slab[:, seq_len:2 * seq_len].astype(jnp.int32)
    plen_all = slab[:, 2 * seq_len]
    tox_all = slab[:, 2 * seq_len + 1]

    live = jnp.arange(seq_len, dtype=jnp.float32)[None, :] >= plen_all[:, None]
    levels = tox_all[:, None] * live.astype(jnp.float32)
    highest = jnp.max(jnp.where(live, grid, -1e30), axis=0)
    expo = jnp.where(live, jnp.exp(jnp.where(live, grid - highest[None, :], -80.0)), 0.0)
    totals = jnp.sum(expo, axis=0)
    lab_sum = jnp.sum(levels, axis=0)
    weights_all = (
        expo / jnp.maximum(totals, 1.0)[None, :] - levels / jnp.maximum(lab_sum, 1.0)[None, :]
    ) / seq_len

    twist_vals = lax.dynamic_index_in_dim(grid, r, axis=0, keepdims=False)
    weights = lax.dynamic_index_in_dim(weights_all, r, axis=0, keepdims=False)

    grad_out = lax.psum(jnp.dot(weights, active, precision=lax.Precision.HIGHEST), "dp")

    slice_len = vocab_size // n_dp
    idx = ids_all.reshape(-1) - r * slice_len
    idx = jnp.where((idx >= 0) & (idx < slice_len), idx, slice_len)
    grad_bias = jnp.zeros((slice_len,), jnp.float32).at[idx].add(
        weights_all.reshape(-1), mode="drop"
    )

    sigma = jax.nn.sigmoid(pre_act)
    d_pre = (
        weights[:, None] * twist_out[None, :] * sigma * (1.0 + pre_act * (1.0 - sigma))
    ).astype(jnp.bfloat16)
    contract = (((0,), (0,)), ((), ()))
    grad_part = lax.dot_general(
        normed, d_pre, contract, preferred_element_type=jnp.float32
    ).astype(jnp.bfloat16)
    hcut = grad_part.shape[1] // SPLITS
    grad_in = jnp.concatenate(
        [
            lax.psum_scatter(
                grad_part[:, s * hcut:(s + 1) * hcut], "dp", scatter_dimension=0, tiled=True
            )
            for s in range(SPLITS)
        ],
        axis=1,
    ).astype(jnp.float32)
    return (twist_vals, grad_in, grad_out, grad_bias)


def solution(mesh):
    placed = (
        P("dp"),
        P("dp", "tensor"),
        P("tensor", None),
        P(("dp", "tensor"), None),
        P(),
        P("dp", "tensor"),
        P("tensor"),
        P(),
        P("dp"),
        P("dp"),
    )
    return jax.shard_map(
        local,
        mesh=mesh,
        in_specs=placed,
        out_specs=(P("dp"), P("dp", "tensor"), P("tensor"), P("dp")),
        check_vma=False,
    )
```

```python
import jax
import jax.numpy as jnp
from jax import lax
from jax.sharding import PartitionSpec as P

SPLITS = 1


def normalize(hidden, norm_gain):
    values = hidden.astype(jnp.float32)
    scaled = lax.rsqrt(jnp.mean(values * values, axis=-1, keepdims=True) + 1e-05)
    return (values * scaled * norm_gain[None, :]).astype(jnp.bfloat16)


def local(
    token_ids,
    attn_heads,
    out_proj,
    residual,
    norm_gain,
    twist_in,
    twist_out,
    token_bias,
    toxicity,
    prompt_len,
):
    seq_len = attn_heads.shape[0]
    width = out_proj.shape[1]
    vocab_size = token_bias.shape[0]
    n_dp = lax.axis_size("dp")
    r = lax.axis_index("dp")
    j = lax.axis_index("tensor")
    rows = residual.shape[0]

    twist_full = lax.all_gather(twist_in, "dp", axis=0, tiled=True)

    resid_pad = lax.dynamic_update_slice(
        jnp.zeros((seq_len, width), residual.dtype), residual, (j * rows, 0)
    )
    partial_sum = jnp.dot(attn_heads, out_proj, preferred_element_type=jnp.float32)
    partial_sum = (partial_sum + resid_pad.astype(jnp.float32)).astype(jnp.bfloat16)
    cut = width // SPLITS
    hidden = jnp.concatenate(
        [lax.psum(partial_sum[:, s * cut:(s + 1) * cut], "tensor") for s in range(SPLITS)],
        axis=1,
    )
    normed = normalize(hidden, norm_gain)

    blk = normed.shape[1] // n_dp
    pieces = [lax.dynamic_slice_in_dim(normed, r * blk, blk, axis=1)]
    for s in range(1, n_dp):
        send = lax.dynamic_slice_in_dim(normed, ((r + s) % n_dp) * blk, blk, axis=1)
        pieces.append(
            lax.ppermute(send, "dp", [(i, (i + s) % n_dp) for i in range(n_dp)])
        )
    by_shift = jnp.stack(pieces)
    order = (r - jnp.arange(n_dp)) % n_dp
    normed_cols = jnp.take(by_shift, order, axis=0).reshape(n_dp * seq_len, blk)

    pre_act = jnp.dot(normed, twist_full, preferred_element_type=jnp.float32)
    active = jax.nn.silu(pre_act)
    partial_psi = jnp.dot(active, twist_out, precision=lax.Precision.HIGHEST)

    lead = (j == 0).astype(jnp.float32)
    own_bias = token_bias[token_ids]
    row = jnp.concatenate(
        [
            partial_psi + lead * own_bias,
            lead * token_ids.astype(jnp.float32),
            lead * prompt_len.astype(jnp.float32),
            lead * toxicity.astype(jnp.float32),
        ]
    )
    slot = (jnp.arange(n_dp) == r).astype(jnp.float32)
    slab = lax.psum(slot[:, None] * row[None, :], ("dp", "tensor"))
    grid = slab[:, :seq_len]
    ids_all = slab[:, seq_len:2 * seq_len].astype(jnp.int32)
    plen_all = slab[:, 2 * seq_len]
    tox_all = slab[:, 2 * seq_len + 1]

    live = jnp.arange(seq_len, dtype=jnp.float32)[None, :] >= plen_all[:, None]
    levels = tox_all[:, None] * live.astype(jnp.float32)
    highest = jnp.max(jnp.where(live, grid, -1e30), axis=0)
    expo = jnp.where(live, jnp.exp(jnp.where(live, grid - highest[None, :], -80.0)), 0.0)
    totals = jnp.sum(expo, axis=0)
    lab_sum = jnp.sum(levels, axis=0)
    weights_all = (
        expo / jnp.maximum(totals, 1.0)[None, :] - levels / jnp.maximum(lab_sum, 1.0)[None, :]
    ) / seq_len

    twist_vals = lax.dynamic_index_in_dim(grid, r, axis=0, keepdims=False)
    weights = lax.dynamic_index_in_dim(weights_all, r, axis=0, keepdims=False)

    slice_len = vocab_size // n_dp
    idx = ids_all.reshape(-1) - r * slice_len
    idx = jnp.where((idx >= 0) & (idx < slice_len), idx, slice_len)
    grad_bias = jnp.zeros((slice_len,), jnp.float32).at[idx].add(
        weights_all.reshape(-1), mode="drop"
    )

    sigma = jax.nn.sigmoid(pre_act)
    d_pre = (
        weights[:, None] * twist_out[None, :] * sigma * (1.0 + pre_act * (1.0 - sigma))
    ).astype(jnp.bfloat16)

    gout = jnp.dot(weights, active, precision=lax.Precision.HIGHEST)
    g_hi = lax.reduce_precision(gout, exponent_bits=8, mantissa_bits=7)
    g_lo = gout - g_hi
    hid = d_pre.shape[1]
    pad = jnp.zeros((14, hid), jnp.bfloat16)
    packed = jnp.concatenate(
        [d_pre, g_hi.astype(jnp.bfloat16)[None], g_lo.astype(jnp.bfloat16)[None], pad]
    )
    gathered = lax.all_gather(packed, "dp", axis=0)
    d_pre_all = gathered[:, :seq_len].reshape(n_dp * seq_len, hid)
    grad_out = jnp.sum(
        gathered[:, seq_len].astype(jnp.float32) + gathered[:, seq_len + 1].astype(jnp.float32),
        axis=0,
    )

    contract = (((0,), (0,)), ((), ()))
    grad_in = lax.dot_general(
        normed_cols, d_pre_all, contract, preferred_element_type=jnp.float32
    )
    return (twist_vals, grad_in, grad_out, grad_bias)


def solution(mesh):
    placed = (
        P("dp"),
        P("dp", "tensor"),
        P("tensor", None),
        P(("dp", "tensor"), None),
        P(),
        P("dp", "tensor"),
        P("tensor"),
        P(),
        P("dp"),
        P("dp"),
    )
    return jax.shard_map(
        local,
        mesh=mesh,
        in_specs=placed,
        out_specs=(P("dp"), P("dp", "tensor"), P("tensor"), P("dp")),
        check_vma=False,
    )
```

```python
import jax
import jax.numpy as jnp
from jax import lax
from jax.sharding import Mesh, PartitionSpec as P

SPLITS = 1


def normalize(hidden, norm_gain):
    values = hidden.astype(jnp.float32)
    scaled = lax.rsqrt(jnp.mean(values * values, axis=-1, keepdims=True) + 1e-05)
    return (values * scaled * norm_gain[None, :]).astype(jnp.bfloat16)


def local(
    token_ids,
    attn_heads,
    out_proj,
    residual,
    norm_gain,
    twist_in,
    twist_out,
    token_bias,
    toxicity,
    prompt_len,
):
    seq_len = attn_heads.shape[0]
    width = out_proj.shape[1]
    vocab_size = token_bias.shape[0]
    n_dp = lax.axis_size("dp")
    r = lax.axis_index("dp")
    j = lax.axis_index(("tz", "tx"))
    rows = residual.shape[0]

    twist_full = lax.all_gather(twist_in, "dp", axis=0, tiled=True)

    resid_pad = lax.dynamic_update_slice(
        jnp.zeros((seq_len, width), residual.dtype), residual, (j * rows, 0)
    )
    partial_sum = jnp.dot(attn_heads, out_proj, preferred_element_type=jnp.float32)
    partial_sum = (partial_sum + resid_pad.astype(jnp.float32)).astype(jnp.bfloat16)
    part = lax.psum_scatter(partial_sum, "tx", scatter_dimension=1, tiled=True)
    part = lax.psum(part, "tz")
    hidden = lax.all_gather(part, "tx", axis=1, tiled=True)
    normed = normalize(hidden, norm_gain)

    pre_act = jnp.dot(normed, twist_full, preferred_element_type=jnp.float32)
    active = jax.nn.silu(pre_act)
    partial_psi = jnp.dot(active, twist_out, precision=lax.Precision.HIGHEST)

    lead = (j == 0).astype(jnp.float32)
    own_bias = token_bias[token_ids]
    row = jnp.concatenate(
        [
            partial_psi + lead * own_bias,
            lead * token_ids.astype(jnp.float32),
            lead * prompt_len.astype(jnp.float32),
            lead * toxicity.astype(jnp.float32),
        ]
    )
    slot = (jnp.arange(n_dp) == r).astype(jnp.float32)
    slab = lax.psum(slot[:, None] * row[None, :], ("dp", "tz", "tx"))
    grid = slab[:, :seq_len]
    ids_all = slab[:, seq_len:2 * seq_len].astype(jnp.int32)
    plen_all = slab[:, 2 * seq_len]
    tox_all = slab[:, 2 * seq_len + 1]

    live = jnp.arange(seq_len, dtype=jnp.float32)[None, :] >= plen_all[:, None]
    levels = tox_all[:, None] * live.astype(jnp.float32)
    highest = jnp.max(jnp.where(live, grid, -1e30), axis=0)
    expo = jnp.where(live, jnp.exp(jnp.where(live, grid - highest[None, :], -80.0)), 0.0)
    totals = jnp.sum(expo, axis=0)
    lab_sum = jnp.sum(levels, axis=0)
    weights_all = (
        expo / jnp.maximum(totals, 1.0)[None, :] - levels / jnp.maximum(lab_sum, 1.0)[None, :]
    ) / seq_len

    twist_vals = lax.dynamic_index_in_dim(grid, r, axis=0, keepdims=False)
    weights = lax.dynamic_index_in_dim(weights_all, r, axis=0, keepdims=False)

    grad_out = lax.psum(jnp.dot(weights, active, precision=lax.Precision.HIGHEST), "dp")

    slice_len = vocab_size // n_dp
    idx = ids_all.reshape(-1) - r * slice_len
    idx = jnp.where((idx >= 0) & (idx < slice_len), idx, slice_len)
    grad_bias = jnp.zeros((slice_len,), jnp.float32).at[idx].add(
        weights_all.reshape(-1), mode="drop"
    )

    sigma = jax.nn.sigmoid(pre_act)
    d_pre = (
        weights[:, None] * twist_out[None, :] * sigma * (1.0 + pre_act * (1.0 - sigma))
    ).astype(jnp.bfloat16)
    contract = (((0,), (0,)), ((), ()))
    grad_part = lax.dot_general(
        normed, d_pre, contract, preferred_element_type=jnp.float32
    ).astype(jnp.bfloat16)
    hcut = grad_part.shape[1] // SPLITS
    grad_in = jnp.concatenate(
        [
            lax.psum_scatter(
                grad_part[:, s * hcut:(s + 1) * hcut], "dp", scatter_dimension=0, tiled=True
            )
            for s in range(SPLITS)
        ],
        axis=1,
    ).astype(jnp.float32)
    return (twist_vals, grad_in, grad_out, grad_bias)


def solution(mesh):
    n_dp, n_tensor = mesh.devices.shape
    n_x = 4
    split = Mesh(mesh.devices.reshape(n_dp, n_tensor // n_x, n_x), ("dp", "tz", "tx"))
    tensor = ("tz", "tx")
    placed = (
        P("dp"),
        P("dp", tensor),
        P(tensor, None),
        P(("dp",) + tensor, None),
        P(),
        P("dp", tensor),
        P(tensor),
        P(),
        P("dp"),
        P("dp"),
    )
    return jax.shard_map(
        local,
        mesh=split,
        in_specs=placed,
        out_specs=(P("dp"), P("dp", tensor), P(tensor), P("dp")),
        check_vma=False,
    )
```

```python
import jax
import jax.numpy as jnp
from jax import lax
from jax.sharding import Mesh, PartitionSpec as P

SPLITS = 1


def normalize(hidden, norm_gain):
    values = hidden.astype(jnp.float32)
    scaled = lax.rsqrt(jnp.mean(values * values, axis=-1, keepdims=True) + 1e-05)
    return (values * scaled * norm_gain[None, :]).astype(jnp.bfloat16)


def local(
    token_ids,
    attn_heads,
    out_proj,
    residual,
    norm_gain,
    twist_in,
    twist_out,
    token_bias,
    toxicity,
    prompt_len,
):
    seq_len = attn_heads.shape[0]
    width = out_proj.shape[1]
    vocab_size = token_bias.shape[0]
    n_dp = lax.axis_size("dp")
    r = lax.axis_index("dp")
    j = lax.axis_index(("tz", "tx"))
    rows = residual.shape[0]

    stack = twist_in[None]
    bits = (2, 3, 1, 0)
    for b in bits:
        got = lax.ppermute(stack, "dp", [(i, i ^ (1 << b)) for i in range(n_dp)])
        stack = jnp.concatenate([stack, got])
    pos = jnp.arange(n_dp)
    want = jnp.zeros((n_dp,), jnp.int32)
    for p_bit in range(len(bits)):
        want = want | ((((pos ^ r) >> bits[p_bit]) & 1) << p_bit)
    twist_full = jnp.take(stack, want, axis=0).reshape(-1, twist_in.shape[1])

    resid_pad = lax.dynamic_update_slice(
        jnp.zeros((seq_len, width), residual.dtype), residual, (j * rows, 0)
    )
    partial_sum = jnp.dot(attn_heads, out_proj, preferred_element_type=jnp.float32)
    partial_sum = (partial_sum + resid_pad.astype(jnp.float32)).astype(jnp.bfloat16)
    part = lax.psum_scatter(partial_sum, "tx", scatter_dimension=1, tiled=True)
    part = lax.psum(part, "tz")
    hidden = lax.all_gather(part, "tx", axis=1, tiled=True)
    normed = normalize(hidden, norm_gain)

    pre_act = jnp.dot(normed, twist_full, preferred_element_type=jnp.float32)
    active = jax.nn.silu(pre_act)
    partial_psi = jnp.dot(active, twist_out, precision=lax.Precision.HIGHEST)

    lead = (j == 0).astype(jnp.float32)
    own_bias = token_bias[token_ids]
    row = jnp.concatenate(
        [
            partial_psi + lead * own_bias,
            lead * token_ids.astype(jnp.float32),
            lead * prompt_len.astype(jnp.float32),
            lead * toxicity.astype(jnp.float32),
        ]
    )
    slot = (jnp.arange(n_dp) == r).astype(jnp.float32)
    slab = lax.psum(slot[:, None] * row[None, :], ("dp", "tz", "tx"))
    grid = slab[:, :seq_len]
    ids_all = slab[:, seq_len:2 * seq_len].astype(jnp.int32)
    plen_all = slab[:, 2 * seq_len]
    tox_all = slab[:, 2 * seq_len + 1]

    live = jnp.arange(seq_len, dtype=jnp.float32)[None, :] >= plen_all[:, None]
    levels = tox_all[:, None] * live.astype(jnp.float32)
    highest = jnp.max(jnp.where(live, grid, -1e30), axis=0)
    expo = jnp.where(live, jnp.exp(jnp.where(live, grid - highest[None, :], -80.0)), 0.0)
    totals = jnp.sum(expo, axis=0)
    lab_sum = jnp.sum(levels, axis=0)
    weights_all = (
        expo / jnp.maximum(totals, 1.0)[None, :] - levels / jnp.maximum(lab_sum, 1.0)[None, :]
    ) / seq_len

    twist_vals = lax.dynamic_index_in_dim(grid, r, axis=0, keepdims=False)
    weights = lax.dynamic_index_in_dim(weights_all, r, axis=0, keepdims=False)

    grad_out = lax.psum(jnp.dot(weights, active, precision=lax.Precision.HIGHEST), "dp")

    slice_len = vocab_size // n_dp
    idx = ids_all.reshape(-1) - r * slice_len
    idx = jnp.where((idx >= 0) & (idx < slice_len), idx, slice_len)
    grad_bias = jnp.zeros((slice_len,), jnp.float32).at[idx].add(
        weights_all.reshape(-1), mode="drop"
    )

    sigma = jax.nn.sigmoid(pre_act)
    d_pre = (
        weights[:, None] * twist_out[None, :] * sigma * (1.0 + pre_act * (1.0 - sigma))
    ).astype(jnp.bfloat16)
    contract = (((0,), (0,)), ((), ()))
    grad_part = lax.dot_general(
        normed, d_pre, contract, preferred_element_type=jnp.float32
    ).astype(jnp.bfloat16)
    hcut = grad_part.shape[1] // SPLITS
    grad_in = jnp.concatenate(
        [
            lax.psum_scatter(
                grad_part[:, s * hcut:(s + 1) * hcut], "dp", scatter_dimension=0, tiled=True
            )
            for s in range(SPLITS)
        ],
        axis=1,
    ).astype(jnp.float32)
    return (twist_vals, grad_in, grad_out, grad_bias)


def solution(mesh):
    n_dp, n_tensor = mesh.devices.shape
    n_x = 4
    split = Mesh(mesh.devices.reshape(n_dp, n_tensor // n_x, n_x), ("dp", "tz", "tx"))
    tensor = ("tz", "tx")
    placed = (
        P("dp"),
        P("dp", tensor),
        P(tensor, None),
        P(("dp",) + tensor, None),
        P(),
        P("dp", tensor),
        P(tensor),
        P(),
        P("dp"),
        P("dp"),
    )
    return jax.shard_map(
        local,
        mesh=split,
        in_specs=placed,
        out_specs=(P("dp"), P("dp", tensor), P(tensor), P("dp")),
        check_vma=False,
    )
```

```python
import jax
import jax.numpy as jnp
from jax import lax
from jax.sharding import Mesh, PartitionSpec as P

SPLITS = 1


def normalize(hidden, norm_gain):
    values = hidden.astype(jnp.float32)
    scaled = lax.rsqrt(jnp.mean(values * values, axis=-1, keepdims=True) + 1e-05)
    return (values * scaled * norm_gain[None, :]).astype(jnp.bfloat16)


def local(
    token_ids,
    attn_heads,
    out_proj,
    residual,
    norm_gain,
    twist_in,
    twist_out,
    token_bias,
    toxicity,
    prompt_len,
):
    seq_len = attn_heads.shape[0]
    width = out_proj.shape[1]
    vocab_size = token_bias.shape[0]
    n_dp = lax.axis_size("dp")
    r = lax.axis_index("dp")
    j = lax.axis_index(("tz", "tx"))
    rows = residual.shape[0]

    stack = twist_in[None]
    bits = (1, 2, 3, 0)
    for b in bits:
        got = lax.ppermute(stack, "dp", [(i, i ^ (1 << b)) for i in range(n_dp)])
        stack = jnp.concatenate([stack, got])
    pos = jnp.arange(n_dp)
    want = jnp.zeros((n_dp,), jnp.int32)
    for p_bit in range(len(bits)):
        want = want | ((((pos ^ r) >> bits[p_bit]) & 1) << p_bit)
    twist_full = jnp.take(stack, want, axis=0).reshape(-1, twist_in.shape[1])

    resid_pad = lax.dynamic_update_slice(
        jnp.zeros((seq_len, width), residual.dtype), residual, (j * rows, 0)
    )
    partial_sum = jnp.dot(attn_heads, out_proj, preferred_element_type=jnp.float32)
    partial_sum = (partial_sum + resid_pad.astype(jnp.float32)).astype(jnp.bfloat16)
    part = lax.psum_scatter(partial_sum, "tx", scatter_dimension=1, tiled=True)
    part = lax.psum(part, "tz")
    hidden = lax.all_gather(part, "tx", axis=1, tiled=True)
    normed = normalize(hidden, norm_gain)

    pre_act = jnp.dot(normed, twist_full, preferred_element_type=jnp.float32)
    active = jax.nn.silu(pre_act)
    partial_psi = jnp.dot(active, twist_out, precision=lax.Precision.HIGHEST)

    lead = (j == 0).astype(jnp.float32)
    own_bias = token_bias[token_ids]
    row = jnp.concatenate(
        [
            partial_psi + lead * own_bias,
            lead * token_ids.astype(jnp.float32),
            lead * prompt_len.astype(jnp.float32),
            lead * toxicity.astype(jnp.float32),
        ]
    )
    slot = (jnp.arange(n_dp) == r).astype(jnp.float32)
    slab = lax.psum(slot[:, None] * row[None, :], ("dp", "tz", "tx"))
    grid = slab[:, :seq_len]
    ids_all = slab[:, seq_len:2 * seq_len].astype(jnp.int32)
    plen_all = slab[:, 2 * seq_len]
    tox_all = slab[:, 2 * seq_len + 1]

    live = jnp.arange(seq_len, dtype=jnp.float32)[None, :] >= plen_all[:, None]
    levels = tox_all[:, None] * live.astype(jnp.float32)
    highest = jnp.max(jnp.where(live, grid, -1e30), axis=0)
    expo = jnp.where(live, jnp.exp(jnp.where(live, grid - highest[None, :], -80.0)), 0.0)
    totals = jnp.sum(expo, axis=0)
    lab_sum = jnp.sum(levels, axis=0)
    weights_all = (
        expo / jnp.maximum(totals, 1.0)[None, :] - levels / jnp.maximum(lab_sum, 1.0)[None, :]
    ) / seq_len

    twist_vals = lax.dynamic_index_in_dim(grid, r, axis=0, keepdims=False)
    weights = lax.dynamic_index_in_dim(weights_all, r, axis=0, keepdims=False)

    grad_out = lax.psum(jnp.dot(weights, active, precision=lax.Precision.HIGHEST), "dp")

    slice_len = vocab_size // n_dp
    idx = ids_all.reshape(-1) - r * slice_len
    idx = jnp.where((idx >= 0) & (idx < slice_len), idx, slice_len)
    grad_bias = jnp.zeros((slice_len,), jnp.float32).at[idx].add(
        weights_all.reshape(-1), mode="drop"
    )

    sigma = jax.nn.sigmoid(pre_act)
    d_pre = (
        weights[:, None] * twist_out[None, :] * sigma * (1.0 + pre_act * (1.0 - sigma))
    ).astype(jnp.bfloat16)
    contract = (((0,), (0,)), ((), ()))
    grad_part = lax.dot_general(
        normed, d_pre, contract, preferred_element_type=jnp.float32
    ).astype(jnp.bfloat16)
    hcut = grad_part.shape[1] // SPLITS
    grad_in = jnp.concatenate(
        [
            lax.psum_scatter(
                grad_part[:, s * hcut:(s + 1) * hcut], "dp", scatter_dimension=0, tiled=True
            )
            for s in range(SPLITS)
        ],
        axis=1,
    ).astype(jnp.float32)
    return (twist_vals, grad_in, grad_out, grad_bias)


def solution(mesh):
    n_dp, n_tensor = mesh.devices.shape
    n_x = 4
    split = Mesh(mesh.devices.reshape(n_dp, n_tensor // n_x, n_x), ("dp", "tz", "tx"))
    tensor = ("tz", "tx")
    placed = (
        P("dp"),
        P("dp", tensor),
        P(tensor, None),
        P(("dp",) + tensor, None),
        P(),
        P("dp", tensor),
        P(tensor),
        P(),
        P("dp"),
        P("dp"),
    )
    return jax.shard_map(
        local,
        mesh=split,
        in_specs=placed,
        out_specs=(P("dp"), P("dp", tensor), P(tensor), P("dp")),
        check_vma=False,
    )
```

```python
import jax
import jax.numpy as jnp
from jax import lax
from jax.sharding import Mesh, PartitionSpec as P

SPLITS = 1


def normalize(hidden, norm_gain):
    values = hidden.astype(jnp.float32)
    scaled = lax.rsqrt(jnp.mean(values * values, axis=-1, keepdims=True) + 1e-05)
    return (values * scaled * norm_gain[None, :]).astype(jnp.bfloat16)


def local(
    token_ids,
    attn_heads,
    out_proj,
    residual,
    norm_gain,
    twist_in,
    twist_out,
    token_bias,
    toxicity,
    prompt_len,
):
    seq_len = attn_heads.shape[0]
    width = out_proj.shape[1]
    vocab_size = token_bias.shape[0]
    n_dp = lax.axis_size("dp")
    r = lax.axis_index("dp")
    j = lax.axis_index(("tz", "tx"))
    rows = residual.shape[0]

    stack = twist_in[None]
    bits = (1, 2, 3, 0)
    for b in bits:
        got = lax.ppermute(stack, "dp", [(i, i ^ (1 << b)) for i in range(n_dp)])
        stack = jnp.concatenate([stack, got])
    pos = jnp.arange(n_dp)
    want = jnp.zeros((n_dp,), jnp.int32)
    for p_bit in range(len(bits)):
        want = want | ((((pos ^ r) >> bits[p_bit]) & 1) << p_bit)
    twist_full = jnp.take(stack, want, axis=0).reshape(-1, twist_in.shape[1])

    resid_pad = lax.dynamic_update_slice(
        jnp.zeros((seq_len, width), residual.dtype), residual, (j * rows, 0)
    )
    partial_sum = jnp.dot(attn_heads, out_proj, preferred_element_type=jnp.float32)
    partial_sum = (partial_sum + resid_pad.astype(jnp.float32)).astype(jnp.bfloat16)
    part = lax.psum_scatter(partial_sum, "tx", scatter_dimension=1, tiled=True)
    part = lax.psum(part, "tz")
    hidden = lax.all_gather(part, "tx", axis=1, tiled=True)
    normed = normalize(hidden, norm_gain)

    pre_act = jnp.dot(normed, twist_full, preferred_element_type=jnp.float32)
    active = jax.nn.silu(pre_act)
    partial_psi = jnp.dot(active, twist_out, precision=lax.Precision.HIGHEST)

    lead = (j == 0).astype(jnp.float32)
    own_bias = token_bias[token_ids]
    row = jnp.concatenate(
        [
            partial_psi + lead * own_bias,
            lead * token_ids.astype(jnp.float32),
            lead * prompt_len.astype(jnp.float32),
            lead * toxicity.astype(jnp.float32),
        ]
    )
    slot = (jnp.arange(n_dp) == r).astype(jnp.float32)
    slab = lax.psum(slot[:, None] * row[None, :], ("dp", "tz", "tx"))
    grid = slab[:, :seq_len]
    ids_all = slab[:, seq_len:2 * seq_len].astype(jnp.int32)
    plen_all = slab[:, 2 * seq_len]
    tox_all = slab[:, 2 * seq_len + 1]

    live = jnp.arange(seq_len, dtype=jnp.float32)[None, :] >= plen_all[:, None]
    levels = tox_all[:, None] * live.astype(jnp.float32)
    highest = jnp.max(jnp.where(live, grid, -1e30), axis=0)
    expo = jnp.where(live, jnp.exp(jnp.where(live, grid - highest[None, :], -80.0)), 0.0)
    totals = jnp.sum(expo, axis=0)
    lab_sum = jnp.sum(levels, axis=0)
    weights_all = (
        expo / jnp.maximum(totals, 1.0)[None, :] - levels / jnp.maximum(lab_sum, 1.0)[None, :]
    ) / seq_len

    twist_vals = lax.dynamic_index_in_dim(grid, r, axis=0, keepdims=False)
    weights = lax.dynamic_index_in_dim(weights_all, r, axis=0, keepdims=False)

    grad_out = lax.psum(jnp.dot(weights, active, precision=lax.Precision.HIGHEST), "dp")

    slice_len = vocab_size // n_dp
    idx = ids_all.reshape(-1) - r * slice_len
    idx = jnp.where((idx >= 0) & (idx < slice_len), idx, slice_len)
    grad_bias = jnp.zeros((slice_len,), jnp.float32).at[idx].add(
        weights_all.reshape(-1), mode="drop"
    )

    sigma = jax.nn.sigmoid(pre_act)
    d_pre = (
        weights[:, None] * twist_out[None, :] * sigma * (1.0 + pre_act * (1.0 - sigma))
    ).astype(jnp.bfloat16)
    contract = (((0,), (0,)), ((), ()))
    grad_part = lax.dot_general(
        normed, d_pre, contract, preferred_element_type=jnp.float32
    ).astype(jnp.bfloat16)
    cols = grad_part.shape[1] // 2
    native = lax.psum_scatter(grad_part[:, :cols], "dp", scatter_dimension=0, tiled=True)
    n_bits = n_dp.bit_length() - 1
    acc = grad_part[:, cols:].astype(jnp.float32).reshape((2,) * n_bits + (-1, cols))
    left = list(range(n_bits - 1, -1, -1))
    for b in (0, 2, 3, 1):
        axis = left.index(b)
        left.remove(b)
        mine = (r >> b) & 1
        keep = lax.dynamic_index_in_dim(acc, mine, axis=axis, keepdims=False)
        send = lax.dynamic_index_in_dim(acc, 1 - mine, axis=axis, keepdims=False)
        got = lax.ppermute(
            send.astype(jnp.bfloat16), "dp", [(i, i ^ (1 << b)) for i in range(n_dp)]
        )
        acc = keep + got.astype(jnp.float32)
    grad_in = jnp.concatenate([native.astype(jnp.float32), acc], axis=1)
    return (twist_vals, grad_in, grad_out, grad_bias)


def solution(mesh):
    n_dp, n_tensor = mesh.devices.shape
    n_x = 4
    split = Mesh(mesh.devices.reshape(n_dp, n_tensor // n_x, n_x), ("dp", "tz", "tx"))
    tensor = ("tz", "tx")
    placed = (
        P("dp"),
        P("dp", tensor),
        P(tensor, None),
        P(("dp",) + tensor, None),
        P(),
        P("dp", tensor),
        P(tensor),
        P(),
        P("dp"),
        P("dp"),
    )
    return jax.shard_map(
        local,
        mesh=split,
        in_specs=placed,
        out_specs=(P("dp"), P("dp", tensor), P(tensor), P("dp")),
        check_vma=False,
    )
```

```python
import jax
import jax.numpy as jnp
from jax import lax
from jax.sharding import Mesh, PartitionSpec as P

SPLITS = 1


def normalize(hidden, norm_gain):
    values = hidden.astype(jnp.float32)
    scaled = lax.rsqrt(jnp.mean(values * values, axis=-1, keepdims=True) + 1e-05)
    return (values * scaled * norm_gain[None, :]).astype(jnp.bfloat16)


def local(
    token_ids,
    attn_heads,
    out_proj,
    residual,
    norm_gain,
    twist_in,
    twist_out,
    token_bias,
    toxicity,
    prompt_len,
):
    seq_len = attn_heads.shape[0]
    width = out_proj.shape[1]
    vocab_size = token_bias.shape[0]
    n_dp = lax.axis_size("dp")
    r = lax.axis_index("dp")
    j = lax.axis_index(("tz", "tx"))
    rows = residual.shape[0]

    stack = twist_in[None]
    bits = (1, 2, 3, 0)
    for b in bits:
        got = lax.ppermute(stack, "dp", [(i, i ^ (1 << b)) for i in range(n_dp)])
        stack = jnp.concatenate([stack, got])
    pos = jnp.arange(n_dp)
    want = jnp.zeros((n_dp,), jnp.int32)
    for p_bit in range(len(bits)):
        want = want | ((((pos ^ r) >> bits[p_bit]) & 1) << p_bit)
    twist_full = jnp.take(stack, want, axis=0).reshape(-1, twist_in.shape[1])

    resid_pad = lax.dynamic_update_slice(
        jnp.zeros((seq_len, width), residual.dtype), residual, (j * rows, 0)
    )
    partial_sum = jnp.dot(attn_heads, out_proj, preferred_element_type=jnp.float32)
    partial_sum = (partial_sum + resid_pad.astype(jnp.float32)).astype(jnp.bfloat16)
    part = lax.psum_scatter(partial_sum, "tx", scatter_dimension=1, tiled=True)
    part = lax.psum(part, "tz")
    hidden = lax.all_gather(part, "tx", axis=1, tiled=True)
    normed = normalize(hidden, norm_gain)

    pre_act = jnp.dot(normed, twist_full, preferred_element_type=jnp.float32)
    active = jax.nn.silu(pre_act)
    partial_psi = jnp.dot(active, twist_out, precision=lax.Precision.HIGHEST)

    lead = (j == 0).astype(jnp.float32)
    own_bias = token_bias[token_ids]
    row = jnp.concatenate(
        [
            partial_psi + lead * own_bias,
            lead * token_ids.astype(jnp.float32),
            lead * prompt_len.astype(jnp.float32),
            lead * toxicity.astype(jnp.float32),
        ]
    )
    slot = (jnp.arange(n_dp) == r).astype(jnp.float32)
    slab = lax.psum(slot[:, None] * row[None, :], ("dp", "tz", "tx"))
    grid = slab[:, :seq_len]
    ids_all = slab[:, seq_len:2 * seq_len].astype(jnp.int32)
    plen_all = slab[:, 2 * seq_len]
    tox_all = slab[:, 2 * seq_len + 1]

    live = jnp.arange(seq_len, dtype=jnp.float32)[None, :] >= plen_all[:, None]
    levels = tox_all[:, None] * live.astype(jnp.float32)
    highest = jnp.max(jnp.where(live, grid, -1e30), axis=0)
    expo = jnp.where(live, jnp.exp(jnp.where(live, grid - highest[None, :], -80.0)), 0.0)
    totals = jnp.sum(expo, axis=0)
    lab_sum = jnp.sum(levels, axis=0)
    weights_all = (
        expo / jnp.maximum(totals, 1.0)[None, :] - levels / jnp.maximum(lab_sum, 1.0)[None, :]
    ) / seq_len

    twist_vals = lax.dynamic_index_in_dim(grid, r, axis=0, keepdims=False)
    weights = lax.dynamic_index_in_dim(weights_all, r, axis=0, keepdims=False)

    grad_out = jnp.dot(weights, active, precision=lax.Precision.HIGHEST)
    for b in (0, 2, 3, 1):
        grad_out = grad_out + lax.ppermute(
            grad_out, "dp", [(i, i ^ (1 << b)) for i in range(n_dp)]
        )

    slice_len = vocab_size // n_dp
    idx = ids_all.reshape(-1) - r * slice_len
    idx = jnp.where((idx >= 0) & (idx < slice_len), idx, slice_len)
    grad_bias = jnp.zeros((slice_len,), jnp.float32).at[idx].add(
        weights_all.reshape(-1), mode="drop"
    )

    sigma = jax.nn.sigmoid(pre_act)
    d_pre = (
        weights[:, None] * twist_out[None, :] * sigma * (1.0 + pre_act * (1.0 - sigma))
    ).astype(jnp.bfloat16)
    contract = (((0,), (0,)), ((), ()))
    grad_part = lax.dot_general(
        normed, d_pre, contract, preferred_element_type=jnp.float32
    ).astype(jnp.bfloat16)
    cols = grad_part.shape[1] // 2
    native = lax.psum_scatter(grad_part[:, :cols], "dp", scatter_dimension=0, tiled=True)
    n_bits = n_dp.bit_length() - 1
    acc = grad_part[:, cols:].astype(jnp.float32).reshape((2,) * n_bits + (-1, cols))
    left = list(range(n_bits - 1, -1, -1))
    for b in (0, 2, 3, 1):
        axis = left.index(b)
        left.remove(b)
        mine = (r >> b) & 1
        keep = lax.dynamic_index_in_dim(acc, mine, axis=axis, keepdims=False)
        send = lax.dynamic_index_in_dim(acc, 1 - mine, axis=axis, keepdims=False)
        got = lax.ppermute(
            send.astype(jnp.bfloat16), "dp", [(i, i ^ (1 << b)) for i in range(n_dp)]
        )
        acc = keep + got.astype(jnp.float32)
    grad_in = jnp.concatenate([native.astype(jnp.float32), acc], axis=1)
    return (twist_vals, grad_in, grad_out, grad_bias)


def solution(mesh):
    n_dp, n_tensor = mesh.devices.shape
    n_x = 4
    split = Mesh(mesh.devices.reshape(n_dp, n_tensor // n_x, n_x), ("dp", "tz", "tx"))
    tensor = ("tz", "tx")
    placed = (
        P("dp"),
        P("dp", tensor),
        P(tensor, None),
        P(("dp",) + tensor, None),
        P(),
        P("dp", tensor),
        P(tensor),
        P(),
        P("dp"),
        P("dp"),
    )
    return jax.shard_map(
        local,
        mesh=split,
        in_specs=placed,
        out_specs=(P("dp"), P("dp", tensor), P(tensor), P("dp")),
        check_vma=False,
    )
```

```python
import jax
import jax.numpy as jnp
from jax import lax
from jax.sharding import Mesh, PartitionSpec as P

SPLITS = 1


def normalize(hidden, norm_gain):
    values = hidden.astype(jnp.float32)
    scaled = lax.rsqrt(jnp.mean(values * values, axis=-1, keepdims=True) + 1e-05)
    return (values * scaled * norm_gain[None, :]).astype(jnp.bfloat16)


def local(
    token_ids,
    attn_heads,
    out_proj,
    residual,
    norm_gain,
    twist_in,
    twist_out,
    token_bias,
    toxicity,
    prompt_len,
):
    seq_len = attn_heads.shape[0]
    width = out_proj.shape[1]
    vocab_size = token_bias.shape[0]
    n_dp = lax.axis_size("dp")
    r = lax.axis_index("dp")
    j = lax.axis_index(("tz", "tx"))
    rows = residual.shape[0]

    stack = twist_in[None]
    bits = (1, 2, 3, 0)
    for b in bits:
        got = lax.ppermute(stack, "dp", [(i, i ^ (1 << b)) for i in range(n_dp)])
        stack = jnp.concatenate([stack, got])
    pos = jnp.arange(n_dp)
    want = jnp.zeros((n_dp,), jnp.int32)
    for p_bit in range(len(bits)):
        want = want | ((((pos ^ r) >> bits[p_bit]) & 1) << p_bit)
    twist_full = jnp.take(stack, want, axis=0).reshape(-1, twist_in.shape[1])

    resid_pad = lax.dynamic_update_slice(
        jnp.zeros((seq_len, width), residual.dtype), residual, (j * rows, 0)
    )
    partial_sum = jnp.dot(attn_heads, out_proj, preferred_element_type=jnp.float32)
    partial_sum = (partial_sum + resid_pad.astype(jnp.float32)).astype(jnp.bfloat16)
    part = lax.psum_scatter(partial_sum, "tx", scatter_dimension=1, tiled=True)
    part = lax.psum(part, "tz")
    hidden = lax.all_gather(part, "tx", axis=1, tiled=True)
    normed = normalize(hidden, norm_gain)

    pre_act = jnp.dot(normed, twist_full, preferred_element_type=jnp.float32)
    active = jax.nn.silu(pre_act)
    partial_psi = jnp.dot(active, twist_out, precision=lax.Precision.HIGHEST)

    lead = (j == 0).astype(jnp.float32)
    own_bias = token_bias[token_ids]
    row = jnp.concatenate(
        [
            partial_psi + lead * own_bias,
            lead * token_ids.astype(jnp.float32),
            lead * prompt_len.astype(jnp.float32),
            lead * toxicity.astype(jnp.float32),
        ]
    )
    slot = (jnp.arange(n_dp) == r).astype(jnp.float32)
    slab = slot[:, None] * row[None, :]
    n_tensor = lax.axis_size(("tz", "tx"))
    for b in range(n_tensor.bit_length() - 1):
        slab = slab + lax.ppermute(
            slab, ("tz", "tx"), [(i, i ^ (1 << b)) for i in range(n_tensor)]
        )
    for b in (0, 2, 3, 1):
        slab = slab + lax.ppermute(slab, "dp", [(i, i ^ (1 << b)) for i in range(n_dp)])
    grid = slab[:, :seq_len]
    ids_all = slab[:, seq_len:2 * seq_len].astype(jnp.int32)
    plen_all = slab[:, 2 * seq_len]
    tox_all = slab[:, 2 * seq_len + 1]

    live = jnp.arange(seq_len, dtype=jnp.float32)[None, :] >= plen_all[:, None]
    levels = tox_all[:, None] * live.astype(jnp.float32)
    highest = jnp.max(jnp.where(live, grid, -1e30), axis=0)
    expo = jnp.where(live, jnp.exp(jnp.where(live, grid - highest[None, :], -80.0)), 0.0)
    totals = jnp.sum(expo, axis=0)
    lab_sum = jnp.sum(levels, axis=0)
    weights_all = (
        expo / jnp.maximum(totals, 1.0)[None, :] - levels / jnp.maximum(lab_sum, 1.0)[None, :]
    ) / seq_len

    twist_vals = lax.dynamic_index_in_dim(grid, r, axis=0, keepdims=False)
    weights = lax.dynamic_index_in_dim(weights_all, r, axis=0, keepdims=False)

    grad_out = jnp.dot(weights, active, precision=lax.Precision.HIGHEST)
    for b in (0, 2, 3, 1):
        grad_out = grad_out + lax.ppermute(
            grad_out, "dp", [(i, i ^ (1 << b)) for i in range(n_dp)]
        )

    slice_len = vocab_size // n_dp
    idx = ids_all.reshape(-1) - r * slice_len
    idx = jnp.where((idx >= 0) & (idx < slice_len), idx, slice_len)
    grad_bias = jnp.zeros((slice_len,), jnp.float32).at[idx].add(
        weights_all.reshape(-1), mode="drop"
    )

    sigma = jax.nn.sigmoid(pre_act)
    d_pre = (
        weights[:, None] * twist_out[None, :] * sigma * (1.0 + pre_act * (1.0 - sigma))
    ).astype(jnp.bfloat16)
    contract = (((0,), (0,)), ((), ()))
    grad_part = lax.dot_general(
        normed, d_pre, contract, preferred_element_type=jnp.float32
    ).astype(jnp.bfloat16)
    cols = grad_part.shape[1] // 2
    native = lax.psum_scatter(grad_part[:, :cols], "dp", scatter_dimension=0, tiled=True)
    n_bits = n_dp.bit_length() - 1
    acc = grad_part[:, cols:].astype(jnp.float32).reshape((2,) * n_bits + (-1, cols))
    left = list(range(n_bits - 1, -1, -1))
    for b in (0, 2, 3, 1):
        axis = left.index(b)
        left.remove(b)
        mine = (r >> b) & 1
        keep = lax.dynamic_index_in_dim(acc, mine, axis=axis, keepdims=False)
        send = lax.dynamic_index_in_dim(acc, 1 - mine, axis=axis, keepdims=False)
        got = lax.ppermute(
            send.astype(jnp.bfloat16), "dp", [(i, i ^ (1 << b)) for i in range(n_dp)]
        )
        acc = keep + got.astype(jnp.float32)
    grad_in = jnp.concatenate([native.astype(jnp.float32), acc], axis=1)
    return (twist_vals, grad_in, grad_out, grad_bias)


def solution(mesh):
    n_dp, n_tensor = mesh.devices.shape
    n_x = 4
    split = Mesh(mesh.devices.reshape(n_dp, n_tensor // n_x, n_x), ("dp", "tz", "tx"))
    tensor = ("tz", "tx")
    placed = (
        P("dp"),
        P("dp", tensor),
        P(tensor, None),
        P(("dp",) + tensor, None),
        P(),
        P("dp", tensor),
        P(tensor),
        P(),
        P("dp"),
        P("dp"),
    )
    return jax.shard_map(
        local,
        mesh=split,
        in_specs=placed,
        out_specs=(P("dp"), P("dp", tensor), P(tensor), P("dp")),
        check_vma=False,
    )
```

```python
import jax
import jax.numpy as jnp
from jax import lax
from jax.sharding import Mesh, PartitionSpec as P

SPLITS = 1


def normalize(hidden, norm_gain):
    values = hidden.astype(jnp.float32)
    scaled = lax.rsqrt(jnp.mean(values * values, axis=-1, keepdims=True) + 1e-05)
    return (values * scaled * norm_gain[None, :]).astype(jnp.bfloat16)


def local(
    token_ids,
    attn_heads,
    out_proj,
    residual,
    norm_gain,
    twist_in,
    twist_out,
    token_bias,
    toxicity,
    prompt_len,
):
    seq_len = attn_heads.shape[0]
    width = out_proj.shape[1]
    vocab_size = token_bias.shape[0]
    n_dp = lax.axis_size("dp")
    r = lax.axis_index("dp")
    j = lax.axis_index(("tz", "tx"))
    rows = residual.shape[0]

    stack = twist_in[None]
    bits = (1, 2, 3, 0)
    for b in bits:
        got = lax.ppermute(stack, "dp", [(i, i ^ (1 << b)) for i in range(n_dp)])
        stack = jnp.concatenate([stack, got])
    pos = jnp.arange(n_dp)
    want = jnp.zeros((n_dp,), jnp.int32)
    for p_bit in range(len(bits)):
        want = want | ((((pos ^ r) >> bits[p_bit]) & 1) << p_bit)
    twist_full = jnp.take(stack, want, axis=0).reshape(-1, twist_in.shape[1])

    resid_pad = lax.dynamic_update_slice(
        jnp.zeros((seq_len, width), residual.dtype), residual, (j * rows, 0)
    )
    partial_sum = jnp.dot(attn_heads, out_proj, preferred_element_type=jnp.float32)
    partial_sum = (partial_sum + resid_pad.astype(jnp.float32)).astype(jnp.bfloat16)
    part = lax.psum_scatter(partial_sum, "tx", scatter_dimension=1, tiled=True)
    n_z = lax.axis_size("tz")
    for b in range(n_z.bit_length() - 1):
        got = lax.ppermute(part, "tz", [(i, i ^ (1 << b)) for i in range(n_z)])
        part = (part.astype(jnp.float32) + got.astype(jnp.float32)).astype(jnp.bfloat16)
    hidden = lax.all_gather(part, "tx", axis=1, tiled=True)
    normed = normalize(hidden, norm_gain)

    pre_act = jnp.dot(normed, twist_full, preferred_element_type=jnp.float32)
    active = jax.nn.silu(pre_act)
    partial_psi = jnp.dot(active, twist_out, precision=lax.Precision.HIGHEST)

    lead = (j == 0).astype(jnp.float32)
    own_bias = token_bias[token_ids]
    row = jnp.concatenate(
        [
            partial_psi + lead * own_bias,
            lead * token_ids.astype(jnp.float32),
            lead * prompt_len.astype(jnp.float32),
            lead * toxicity.astype(jnp.float32),
        ]
    )
    slot = (jnp.arange(n_dp) == r).astype(jnp.float32)
    slab = slot[:, None] * row[None, :]
    n_tensor = lax.axis_size(("tz", "tx"))
    for b in range(n_tensor.bit_length() - 1):
        slab = slab + lax.ppermute(
            slab, ("tz", "tx"), [(i, i ^ (1 << b)) for i in range(n_tensor)]
        )
    for b in (0, 2, 3, 1):
        slab = slab + lax.ppermute(slab, "dp", [(i, i ^ (1 << b)) for i in range(n_dp)])
    grid = slab[:, :seq_len]
    ids_all = slab[:, seq_len:2 * seq_len].astype(jnp.int32)
    plen_all = slab[:, 2 * seq_len]
    tox_all = slab[:, 2 * seq_len + 1]

    live = jnp.arange(seq_len, dtype=jnp.float32)[None, :] >= plen_all[:, None]
    levels = tox_all[:, None] * live.astype(jnp.float32)
    highest = jnp.max(jnp.where(live, grid, -1e30), axis=0)
    expo = jnp.where(live, jnp.exp(jnp.where(live, grid - highest[None, :], -80.0)), 0.0)
    totals = jnp.sum(expo, axis=0)
    lab_sum = jnp.sum(levels, axis=0)
    weights_all = (
        expo / jnp.maximum(totals, 1.0)[None, :] - levels / jnp.maximum(lab_sum, 1.0)[None, :]
    ) / seq_len

    twist_vals = lax.dynamic_index_in_dim(grid, r, axis=0, keepdims=False)
    weights = lax.dynamic_index_in_dim(weights_all, r, axis=0, keepdims=False)

    grad_out = jnp.dot(weights, active, precision=lax.Precision.HIGHEST)
    for b in (0, 2, 3, 1):
        grad_out = grad_out + lax.ppermute(
            grad_out, "dp", [(i, i ^ (1 << b)) for i in range(n_dp)]
        )

    slice_len = vocab_size // n_dp
    idx = ids_all.reshape(-1) - r * slice_len
    idx = jnp.where((idx >= 0) & (idx < slice_len), idx, slice_len)
    grad_bias = jnp.zeros((slice_len,), jnp.float32).at[idx].add(
        weights_all.reshape(-1), mode="drop"
    )

    sigma = jax.nn.sigmoid(pre_act)
    d_pre = (
        weights[:, None] * twist_out[None, :] * sigma * (1.0 + pre_act * (1.0 - sigma))
    ).astype(jnp.bfloat16)
    contract = (((0,), (0,)), ((), ()))
    grad_part = lax.dot_general(
        normed, d_pre, contract, preferred_element_type=jnp.float32
    ).astype(jnp.bfloat16)
    cols = grad_part.shape[1] // 2
    native = lax.psum_scatter(grad_part[:, :cols], "dp", scatter_dimension=0, tiled=True)
    n_bits = n_dp.bit_length() - 1
    acc = grad_part[:, cols:].astype(jnp.float32).reshape((2,) * n_bits + (-1, cols))
    left = list(range(n_bits - 1, -1, -1))
    for b in (0, 2, 3, 1):
        axis = left.index(b)
        left.remove(b)
        mine = (r >> b) & 1
        keep = lax.dynamic_index_in_dim(acc, mine, axis=axis, keepdims=False)
        send = lax.dynamic_index_in_dim(acc, 1 - mine, axis=axis, keepdims=False)
        got = lax.ppermute(
            send.astype(jnp.bfloat16), "dp", [(i, i ^ (1 << b)) for i in range(n_dp)]
        )
        acc = keep + got.astype(jnp.float32)
    grad_in = jnp.concatenate([native.astype(jnp.float32), acc], axis=1)
    return (twist_vals, grad_in, grad_out, grad_bias)


def solution(mesh):
    n_dp, n_tensor = mesh.devices.shape
    n_x = 4
    split = Mesh(mesh.devices.reshape(n_dp, n_tensor // n_x, n_x), ("dp", "tz", "tx"))
    tensor = ("tz", "tx")
    placed = (
        P("dp"),
        P("dp", tensor),
        P(tensor, None),
        P(("dp",) + tensor, None),
        P(),
        P("dp", tensor),
        P(tensor),
        P(),
        P("dp"),
        P("dp"),
    )
    return jax.shard_map(
        local,
        mesh=split,
        in_specs=placed,
        out_specs=(P("dp"), P("dp", tensor), P(tensor), P("dp")),
        check_vma=False,
    )
```

```python
import jax
import jax.numpy as jnp
from jax import lax
from jax.sharding import Mesh, PartitionSpec as P

SPLITS = 1


def normalize(hidden, norm_gain):
    values = hidden.astype(jnp.float32)
    scaled = lax.rsqrt(jnp.mean(values * values, axis=-1, keepdims=True) + 1e-05)
    return (values * scaled * norm_gain[None, :]).astype(jnp.bfloat16)


def local(
    token_ids,
    attn_heads,
    out_proj,
    residual,
    norm_gain,
    twist_in,
    twist_out,
    token_bias,
    toxicity,
    prompt_len,
):
    seq_len = attn_heads.shape[0]
    width = out_proj.shape[1]
    vocab_size = token_bias.shape[0]
    n_dp = lax.axis_size("dp")
    r = lax.axis_index("dp")
    j = lax.axis_index(("tz", "tx"))
    rows = residual.shape[0]

    stack = twist_in[None]
    bits = (1, 2, 3, 0)
    for b in bits:
        got = lax.ppermute(stack, "dp", [(i, i ^ (1 << b)) for i in range(n_dp)])
        stack = jnp.concatenate([stack, got])
    pos = jnp.arange(n_dp)
    want = jnp.zeros((n_dp,), jnp.int32)
    for p_bit in range(len(bits)):
        want = want | ((((pos ^ r) >> bits[p_bit]) & 1) << p_bit)
    twist_full = jnp.take(stack, want, axis=0).reshape(-1, twist_in.shape[1])

    resid_pad = lax.dynamic_update_slice(
        jnp.zeros((seq_len, width), residual.dtype), residual, (j * rows, 0)
    )
    partial_sum = jnp.dot(attn_heads, out_proj, preferred_element_type=jnp.float32)
    partial_sum = (partial_sum + resid_pad.astype(jnp.float32)).astype(jnp.bfloat16)
    part = lax.psum_scatter(partial_sum, "tx", scatter_dimension=1, tiled=True)
    part = lax.psum(part, "tz")
    hidden = lax.all_gather(part, "tx", axis=1, tiled=True)
    normed = normalize(hidden, norm_gain)

    pre_act = jnp.dot(normed, twist_full, preferred_element_type=jnp.float32)
    active = jax.nn.silu(pre_act)
    partial_psi = jnp.dot(active, twist_out, precision=lax.Precision.HIGHEST)

    lead = (j == 0).astype(jnp.float32)
    own_bias = token_bias[token_ids]
    row = jnp.concatenate(
        [
            partial_psi + lead * own_bias,
            lead * token_ids.astype(jnp.float32),
            lead * prompt_len.astype(jnp.float32),
            lead * toxicity.astype(jnp.float32),
        ]
    )
    slot = (jnp.arange(n_dp) == r).astype(jnp.float32)
    slab = slot[:, None] * row[None, :]
    n_tensor = lax.axis_size(("tz", "tx"))
    for b in range(n_tensor.bit_length() - 1):
        slab = slab + lax.ppermute(
            slab, ("tz", "tx"), [(i, i ^ (1 << b)) for i in range(n_tensor)]
        )
    for b in (0, 2, 3, 1):
        slab = slab + lax.ppermute(slab, "dp", [(i, i ^ (1 << b)) for i in range(n_dp)])
    grid = slab[:, :seq_len]
    ids_all = slab[:, seq_len:2 * seq_len].astype(jnp.int32)
    plen_all = slab[:, 2 * seq_len]
    tox_all = slab[:, 2 * seq_len + 1]

    live = jnp.arange(seq_len, dtype=jnp.float32)[None, :] >= plen_all[:, None]
    levels = tox_all[:, None] * live.astype(jnp.float32)
    highest = jnp.max(jnp.where(live, grid, -1e30), axis=0)
    expo = jnp.where(live, jnp.exp(jnp.where(live, grid - highest[None, :], -80.0)), 0.0)
    totals = jnp.sum(expo, axis=0)
    lab_sum = jnp.sum(levels, axis=0)
    weights_all = (
        expo / jnp.maximum(totals, 1.0)[None, :] - levels / jnp.maximum(lab_sum, 1.0)[None, :]
    ) / seq_len

    twist_vals = lax.dynamic_index_in_dim(grid, r, axis=0, keepdims=False)
    weights = lax.dynamic_index_in_dim(weights_all, r, axis=0, keepdims=False)

    grad_out = jnp.dot(weights, active, precision=lax.Precision.HIGHEST)
    for b in (0, 2, 3, 1):
        grad_out = grad_out + lax.ppermute(
            grad_out, "dp", [(i, i ^ (1 << b)) for i in range(n_dp)]
        )

    slice_len = vocab_size // n_dp
    idx = ids_all.reshape(-1) - r * slice_len
    idx = jnp.where((idx >= 0) & (idx < slice_len), idx, slice_len)
    grad_bias = jnp.zeros((slice_len,), jnp.float32).at[idx].add(
        weights_all.reshape(-1), mode="drop"
    )

    sigma = jax.nn.sigmoid(pre_act)
    d_pre = (
        weights[:, None] * twist_out[None, :] * sigma * (1.0 + pre_act * (1.0 - sigma))
    ).astype(jnp.bfloat16)
    contract = (((0,), (0,)), ((), ()))
    grad_part = lax.dot_general(
        normed, d_pre, contract, preferred_element_type=jnp.float32
    ).astype(jnp.bfloat16)
    cols = grad_part.shape[1] * 3 // 8
    native = lax.psum_scatter(grad_part[:, :cols], "dp", scatter_dimension=0, tiled=True)
    n_bits = n_dp.bit_length() - 1
    acc = grad_part[:, cols:].astype(jnp.float32).reshape((2,) * n_bits + (-1, grad_part.shape[1] - cols))
    left = list(range(n_bits - 1, -1, -1))
    for b in (0, 2, 3, 1):
        axis = left.index(b)
        left.remove(b)
        mine = (r >> b) & 1
        keep = lax.dynamic_index_in_dim(acc, mine, axis=axis, keepdims=False)
        send = lax.dynamic_index_in_dim(acc, 1 - mine, axis=axis, keepdims=False)
        got = lax.ppermute(
            send.astype(jnp.bfloat16), "dp", [(i, i ^ (1 << b)) for i in range(n_dp)]
        )
        acc = keep + got.astype(jnp.float32)
    grad_in = jnp.concatenate([native.astype(jnp.float32), acc], axis=1)
    return (twist_vals, grad_in, grad_out, grad_bias)


def solution(mesh):
    n_dp, n_tensor = mesh.devices.shape
    n_x = 4
    split = Mesh(mesh.devices.reshape(n_dp, n_tensor // n_x, n_x), ("dp", "tz", "tx"))
    tensor = ("tz", "tx")
    placed = (
        P("dp"),
        P("dp", tensor),
        P(tensor, None),
        P(("dp",) + tensor, None),
        P(),
        P("dp", tensor),
        P(tensor),
        P(),
        P("dp"),
        P("dp"),
    )
    return jax.shard_map(
        local,
        mesh=split,
        in_specs=placed,
        out_specs=(P("dp"), P("dp", tensor), P(tensor), P("dp")),
        check_vma=False,
    )
```
